512 devices in a mesh: seq: 128 (over x, z_hi, y, core), tp: 4 (over z_lo).
Axes of the slice: x: 4, y: 8, z: 8 (z_hi: 2, z_lo: 4; z = z_hi * 4 + z_lo), core: 2. Of those that a mesh axis runs over, the one named last changes fastest.
Arguments:
- queries: bfloat16 [16384, 4096], P('seq', 'tp'), may hold values from -6 to 6
- suffix_entries: bfloat16 [16384, 4096], P('seq', 'tp'), may hold values from -6 to 6
- prefix_cache: bfloat16 [2048, 4096], P(('seq', 'tp')), may hold values from -6 to 6
- block_prefix: int32 [512], replicated, may hold values from 0 to 1, as said below
- request_lengths: int32 [512], P('seq'), may hold values from 0 to 128, as said below
- request_prefix: int32 [512], P('seq'), may hold values from 0 to 1
Outputs:
- attended: bfloat16 [16384, 4096], P('seq', 'tp')
The draws below stay inside these ranges and needn't reach their ends.
Inputs may be any that keep to these rules, and one draw needn't show every extreme that they name: `request_lengths`: the lengths of one index of seq's requests sum to at most 128; at some index they sum to exactly 128, and there one request alone takes all 128 slots. `block_prefix`: exactly half of the blocks belong to each prefix.
All inputs are finite; a program needn't handle non-finite values.
Results may differ from the reference program's by a relative error of at most 0.0049.
Values may be sent and summed in bfloat16 or wider, within the bound.
No kernel may reach another device: no remote copies, remote signals or barrier semaphores. Data moves between devices by JAX's collectives and lax.ppermute only.
A program may use at most 64 MiB of HBM per device.

```python
import math
import jax
import jax.numpy as jnp
from jax import lax

HEADS = 16
HEAD = 128
TOK_DEV = 128
REQ_DEV = 4
PRE_DEV = 4
TOKENS = 16384
REQS = 512
BLOCKS = 512
CACHE = 2048
N_SEQ = 128


def keyvalue_rows(key, salt, row_count):
    inner = jax.random.fold_in(key, salt)
    shape = (row_count, HEADS, 1, HEAD)
    key_part = jnp.clip(2.0 * jax.random.normal(jax.random.fold_in(inner, 1), shape, jnp.float32), -6.0, 6.0)
    value_part = jnp.clip(jax.random.normal(jax.random.fold_in(inner, 2), shape, jnp.float32), -6.0, 6.0)
    joined = jnp.concatenate([key_part, value_part], axis=2)
    return joined.reshape(row_count, HEADS * 2 * HEAD).astype(jnp.bfloat16)


def draw_queries(key, part):
    column_count = 2 * HEADS * HEAD
    drawn = jnp.clip(jax.random.normal(jax.random.fold_in(key, 3), (TOKENS, column_count), jnp.float32), -6.0, 6.0)
    return drawn.astype(jnp.bfloat16)


def draw_suffix_entries(key, part):
    return keyvalue_rows(key, 5, TOKENS)


def draw_prefix_cache(key, part):
    return keyvalue_rows(key, 6, CACHE)


def draw_block_prefix(key, part):
    order = jax.random.permutation(jax.random.fold_in(key, 21), BLOCKS)
    return (order >= BLOCKS // 2).astype(jnp.int32)


def draw_request_lengths(key, part):
    devices = REQS // REQ_DEV
    inner = jax.random.fold_in(key, 31)
    divisor = jax.random.randint(jax.random.fold_in(inner, 1), (devices,), 1, 5)
    jitter = jax.random.randint(jax.random.fold_in(inner, 2), (devices,), 0, TOK_DEV // 8 + 1)
    live_count = jnp.maximum(TOK_DEV // divisor - jitter, 1)
    fullest = jax.random.randint(jax.random.fold_in(inner, 3), (), 0, devices)
    is_fullest = jnp.arange(devices) == fullest
    live_count = jnp.where(is_fullest, TOK_DEV, live_count)
    cuts = jax.random.randint(jax.random.fold_in(inner, 4), (devices, REQ_DEV - 1), 0, TOK_DEV + 1)
    cuts = jnp.sort(cuts * live_count[:, None] // TOK_DEV, axis=1)
    cuts = jnp.where(is_fullest[:, None], 0, cuts)
    edges = jnp.concatenate([jnp.zeros((devices, 1), jnp.int32), cuts.astype(jnp.int32), live_count[:, None].astype(jnp.int32)], axis=1)
    return (edges[:, 1:] - edges[:, :-1]).reshape(REQS).astype(jnp.int32)


def place_ends(values, stream_key, smallest, largest):
    dims = values.shape
    spot = [jax.random.randint(jax.random.fold_in(stream_key, axis), (), 0, dims[axis]) for axis in range(len(dims))]
    values = values.at[tuple(spot)].set(smallest)
    longest = dims.index(max(dims))
    spot[longest] = (spot[longest] + 1) % dims[longest]
    return values.at[tuple(spot)].set(largest)


def setup_inputs(seed: int = 0) -> dict:
    arg_keys = jax.random.split(jax.random.key(seed), 7)
    queries = draw_queries(jax.random.fold_in(arg_keys[6], 71), 0)
    suffix_entries = draw_suffix_entries(jax.random.fold_in(arg_keys[6], 71), 0)
    prefix_cache = draw_prefix_cache(jax.random.fold_in(arg_keys[6], 71), 0)
    block_prefix = draw_block_prefix(jax.random.fold_in(arg_keys[6], 71), 0)
    request_lengths = draw_request_lengths(jax.random.fold_in(arg_keys[6], 71), 0)
    request_prefix = place_ends(jax.random.randint(arg_keys[5], (REQS,), 0, 2), jax.random.fold_in(arg_keys[5], 1), 0, 1).astype(jnp.int32)
    return dict(queries=queries, suffix_entries=suffix_entries, prefix_cache=prefix_cache, block_prefix=block_prefix, request_lengths=request_lengths, request_prefix=request_prefix)


masked_score = -1e+30

def token_layout(lengths, prefixes, slots):
    cumulative = jnp.cumsum(lengths).astype(jnp.int32)
    slot_ids = jnp.arange(slots, dtype=jnp.int32)
    request_ids = lax.optimization_barrier(jnp.sum((slot_ids[:, None] >= cumulative[None, :]).astype(jnp.int32), axis=1)).astype(jnp.int32)
    live_slots = slot_ids < cumulative[-1]
    onehot = request_ids[:, None] == jnp.arange(lengths.shape[0], dtype=jnp.int32)[None, :]
    token_group = lax.optimization_barrier(jnp.sum(jnp.where(onehot, prefixes[None, :], 0), axis=1)).astype(jnp.int32)
    return (slot_ids, request_ids, live_slots, token_group)

def reference(queries, suffix_entries, prefix_cache, block_prefix, request_lengths, request_prefix):
    score_scale = 1.0 / math.sqrt(HEAD)
    cache_rows = prefix_cache.reshape(CACHE, HEADS, 2, HEAD).astype(jnp.float32)
    cache_keys = cache_rows[:, :, 0]
    cache_values = cache_rows[:, :, 1]
    position_group = jnp.repeat(block_prefix, PRE_DEV)

    def one_device(index):
        begin = (index * TOK_DEV).astype(jnp.int32)
        query_rows = lax.dynamic_slice_in_dim(queries, begin, TOK_DEV, 0).reshape(TOK_DEV, HEADS, 2, HEAD).astype(jnp.float32)
        own_rows = lax.dynamic_slice_in_dim(suffix_entries, begin, TOK_DEV, 0).reshape(TOK_DEV, HEADS, 2, HEAD).astype(jnp.float32)
        lengths = lax.dynamic_slice_in_dim(request_lengths, (index * REQ_DEV).astype(jnp.int32), REQ_DEV, 0)
        prefixes = lax.dynamic_slice_in_dim(request_prefix, (index * REQ_DEV).astype(jnp.int32), REQ_DEV, 0)
        slot_ids, request_ids, live_slots, token_group = token_layout(lengths, prefixes, TOK_DEV)
        prefix_scores = jnp.einsum('thed,phd->thep', query_rows, cache_keys) * score_scale
        suffix_scores = jnp.einsum('thed,uhd->theu', query_rows, own_rows[:, :, 0]) * score_scale
        prefix_allowed = ((token_group[:, None] == position_group[None, :]) & live_slots[:, None])[:, None, None, :]
        suffix_allowed = ((request_ids[:, None] == request_ids[None, :]) & (slot_ids[None, :] <= slot_ids[:, None]) & live_slots[:, None])[:, None, None, :]
        prefix_scores = jnp.where(prefix_allowed, prefix_scores, masked_score)
        suffix_scores = jnp.where(suffix_allowed, suffix_scores, masked_score)
        row_max = jnp.maximum(lax.optimization_barrier(jnp.max(prefix_scores, axis=-1)), lax.optimization_barrier(jnp.max(suffix_scores, axis=-1)))
        prefix_weight = jnp.where(prefix_allowed, jnp.exp(prefix_scores - row_max[..., None]), 0.0)
        suffix_weight = jnp.where(suffix_allowed, jnp.exp(suffix_scores - row_max[..., None]), 0.0)
        total_weight = lax.optimization_barrier(jnp.sum(prefix_weight, axis=-1)) + lax.optimization_barrier(jnp.sum(suffix_weight, axis=-1))
        prefix_round = lax.optimization_barrier(prefix_weight.astype(jnp.bfloat16)).astype(jnp.float32)
        suffix_round = lax.optimization_barrier(suffix_weight.astype(jnp.bfloat16)).astype(jnp.float32)
        weighted = jnp.einsum('thep,phd->thed', prefix_round, cache_values)
        weighted = weighted + jnp.einsum('theu,uhd->thed', suffix_round, own_rows[:, :, 1])
        live_grid = live_slots[:, None, None]
        safe_total = jnp.where(live_grid, total_weight, 1.0)
        result = jnp.where(live_grid[..., None], weighted / safe_total[..., None], 0.0)
        return result.astype(jnp.bfloat16).reshape(TOK_DEV, HEADS * 2 * HEAD)
    blocks = lax.map(one_device, jnp.arange(N_SEQ, dtype=jnp.int32))
    return blocks.reshape(TOKENS, HEADS * 2 * HEAD)
```

```python
import math

import jax
import jax.numpy as jnp
import numpy as np
from jax import lax
from jax.sharding import Mesh
from jax.sharding import PartitionSpec as P

HEADS = 16
HEAD = 128

masked_score = -1e30

SEQ_PARTS = (("x", 4), ("zh", 2), ("y", 8), ("core", 2))
STAGES = (("x", "zh", "y"), ("core",))
TP_FIRST = "a2a"


def block_table(stages, per_block_rows, tensor_count):
    names = [n for n, _ in SEQ_PARTS]
    sizes = [s for _, s in SEQ_PARTS]
    coords = np.indices(sizes).reshape(len(sizes), -1).T
    seq_index = np.ravel_multi_index(coords.T, sizes)
    local = {}
    for c, s in zip(map(tuple, coords), seq_index):
        blocks = s * tensor_count + np.arange(tensor_count)
        local[c] = np.repeat(blocks, per_block_rows)
    gathered = set()
    for stage in stages:
        axes = [names.index(n) for n in stage]
        new = {}
        for c in local:
            parts = []
            for sub in np.ndindex(*[sizes[a] for a in axes]):
                other = list(c)
                for a, v in zip(axes, sub):
                    other[a] = v
                parts.append(local[tuple(other)])
            new[c] = np.concatenate(parts)
        local = new
        gathered.update(stage)
    tables = {tuple(v) for v in local.values()}
    assert len(tables) == 1
    return np.asarray(tables.pop(), np.int32)


def token_layout(lengths, prefixes, slots):
    cumulative = jnp.cumsum(lengths)
    slot_ids = jnp.arange(slots, dtype=jnp.int32)
    request_ids = jnp.sum((slot_ids[:, None] >= cumulative[None, :]).astype(jnp.int32), axis=1)
    live_slots = slot_ids < cumulative[-1]
    onehot = request_ids[:, None] == jnp.arange(lengths.shape[0], dtype=jnp.int32)[None, :]
    token_group = jnp.sum(jnp.where(onehot, prefixes[None, :], 0), axis=1)
    return (slot_ids, request_ids, live_slots, token_group)


def per_device(
    queries, suffix_entries, prefix_cache, block_prefix, request_lengths, request_prefix
):
    tensor_count = lax.axis_size("tp")
    local_heads = HEADS // tensor_count
    token_rows = queries.shape[0]
    block_rows = prefix_cache.shape[0]
    column_count = prefix_cache.shape[1] // tensor_count
    slot_ids, request_ids, live_slots, token_group = token_layout(
        request_lengths, request_prefix, token_rows
    )
    if TP_FIRST == "a2a":
        mine = lax.all_to_all(prefix_cache, "tp", split_axis=1, concat_axis=0, tiled=True)
    else:
        whole = lax.all_gather(prefix_cache, "tp", axis=0, tiled=True)
        start = lax.axis_index("tp") * column_count
        mine = lax.dynamic_slice_in_dim(whole, start, column_count, 1)
    for stage in STAGES:
        mine = lax.all_gather(mine, stage, axis=0, tiled=True)
    cached = mine.reshape(-1, local_heads, 2, HEAD)
    table = jnp.asarray(block_table(STAGES, block_rows, tensor_count))
    owners = jnp.take(block_prefix, table)

    query_rows = queries.reshape(token_rows, local_heads, 2, HEAD)
    own_entries = suffix_entries.reshape(token_rows, local_heads, 2, HEAD)
    scale = 1.0 / math.sqrt(HEAD)
    prefix_scores = jnp.einsum(
        "thed,phd->thep", query_rows, cached[:, :, 0], preferred_element_type=jnp.float32
    ) * scale
    suffix_scores = jnp.einsum(
        "thed,uhd->theu", query_rows, own_entries[:, :, 0], preferred_element_type=jnp.float32
    ) * scale
    prefix_allowed = ((token_group[:, None] == owners[None, :]) & live_slots[:, None])[:, None, None, :]
    suffix_allowed = (
        (request_ids[:, None] == request_ids[None, :])
        & (slot_ids[None, :] <= slot_ids[:, None])
        & live_slots[:, None]
    )[:, None, None, :]
    prefix_scores = jnp.where(prefix_allowed, prefix_scores, masked_score)
    suffix_scores = jnp.where(suffix_allowed, suffix_scores, masked_score)
    row_max = jnp.maximum(jnp.max(prefix_scores, axis=-1), jnp.max(suffix_scores, axis=-1))
    prefix_weight = jnp.where(prefix_allowed, jnp.exp(prefix_scores - row_max[..., None]), 0.0)
    suffix_weight = jnp.where(suffix_allowed, jnp.exp(suffix_scores - row_max[..., None]), 0.0)
    total_weight = jnp.sum(prefix_weight, axis=-1) + jnp.sum(suffix_weight, axis=-1)
    weighted = jnp.einsum(
        "thep,phd->thed", prefix_weight.astype(jnp.bfloat16), cached[:, :, 1],
        preferred_element_type=jnp.float32,
    )
    weighted = weighted + jnp.einsum(
        "theu,uhd->thed", suffix_weight.astype(jnp.bfloat16), own_entries[:, :, 1],
        preferred_element_type=jnp.float32,
    )
    live_grid = live_slots[:, None, None]
    safe_total = jnp.where(live_grid, total_weight, 1.0)
    result = jnp.where(live_grid[..., None], weighted / safe_total[..., None], 0.0)
    return result.astype(jnp.bfloat16).reshape(token_rows, local_heads * 2 * HEAD)


def solution(mesh):
    sizes = tuple(s for _, s in SEQ_PARTS) + (mesh.shape["tp"],)
    names = tuple(n for n, _ in SEQ_PARTS) + ("tp",)
    fine = Mesh(mesh.devices.reshape(sizes), names)
    seq = names[:-1]
    in_specs = (P(seq, "tp"), P(seq, "tp"), P(seq + ("tp",), None), P(), P(seq), P(seq))
    out_specs = P(seq, "tp")
    return jax.shard_map(
        per_device, mesh=fine, in_specs=in_specs, out_specs=out_specs, check_vma=False
    )
```

```python
import math

import jax
import jax.numpy as jnp
import numpy as np
from jax import lax
from jax.sharding import Mesh
from jax.sharding import PartitionSpec as P

HEADS = 16
HEAD = 128

masked_score = -1e30

SEQ_PARTS = (("x", 4), ("zh", 2), ("y", 8), ("core", 2))


def gather_cache(prefix_cache, block_prefix, tensor_count):
    block_rows, width = prefix_cache.shape
    column_count = width // tensor_count
    far = ("x", "zh", "y", "tp")
    peers = 1
    for name, size in SEQ_PARTS:
        if name != "core":
            peers *= size
    parts = prefix_cache.reshape(block_rows, tensor_count, column_count).transpose(1, 0, 2)
    outgoing = jnp.broadcast_to(parts[None], (peers,) + parts.shape).reshape(-1, column_count)
    mine = lax.all_to_all(outgoing, far, split_axis=0, concat_axis=0, tiled=True)
    other = lax.ppermute(mine, "core", [(0, 1), (1, 0)])
    sizes = [s for _, s in SEQ_PARTS] + [tensor_count]
    grid = block_prefix.reshape(sizes)
    core = lax.axis_index("core")
    core_axis = [n for n, _ in SEQ_PARTS].index("core")
    own_owner = jnp.take(grid, core, axis=core_axis).reshape(-1)
    other_owner = jnp.take(grid, 1 - core, axis=core_axis).reshape(-1)
    owners = jnp.repeat(jnp.concatenate([own_owner, other_owner]), block_rows)
    cached = jnp.concatenate([mine, other])
    return cached, owners


def token_layout(lengths, prefixes, slots):
    cumulative = jnp.cumsum(lengths)
    slot_ids = jnp.arange(slots, dtype=jnp.int32)
    request_ids = jnp.sum((slot_ids[:, None] >= cumulative[None, :]).astype(jnp.int32), axis=1)
    live_slots = slot_ids < cumulative[-1]
    onehot = request_ids[:, None] == jnp.arange(lengths.shape[0], dtype=jnp.int32)[None, :]
    token_group = jnp.sum(jnp.where(onehot, prefixes[None, :], 0), axis=1)
    return (slot_ids, request_ids, live_slots, token_group)


def per_device(
    queries, suffix_entries, prefix_cache, block_prefix, request_lengths, request_prefix
):
    tensor_count = lax.axis_size("tp")
    local_heads = HEADS // tensor_count
    token_rows = queries.shape[0]
    block_rows = prefix_cache.shape[0]
    column_count = prefix_cache.shape[1] // tensor_count
    slot_ids, request_ids, live_slots, token_group = token_layout(
        request_lengths, request_prefix, token_rows
    )
    cached, owners = gather_cache(prefix_cache, block_prefix, tensor_count)
    cached = cached.reshape(-1, local_heads, 2, HEAD)

    query_rows = queries.reshape(token_rows, local_heads, 2, HEAD)
    own_entries = suffix_entries.reshape(token_rows, local_heads, 2, HEAD)
    scale = 1.0 / math.sqrt(HEAD)
    prefix_scores = jnp.einsum(
        "thed,phd->thep", query_rows, cached[:, :, 0], preferred_element_type=jnp.float32
    ) * scale
    suffix_scores = jnp.einsum(
        "thed,uhd->theu", query_rows, own_entries[:, :, 0], preferred_element_type=jnp.float32
    ) * scale
    prefix_allowed = ((token_group[:, None] == owners[None, :]) & live_slots[:, None])[:, None, None, :]
    suffix_allowed = (
        (request_ids[:, None] == request_ids[None, :])
        & (slot_ids[None, :] <= slot_ids[:, None])
        & live_slots[:, None]
    )[:, None, None, :]
    prefix_scores = jnp.where(prefix_allowed, prefix_scores, masked_score)
    suffix_scores = jnp.where(suffix_allowed, suffix_scores, masked_score)
    row_max = jnp.maximum(jnp.max(prefix_scores, axis=-1), jnp.max(suffix_scores, axis=-1))
    prefix_weight = jnp.where(prefix_allowed, jnp.exp(prefix_scores - row_max[..., None]), 0.0)
    suffix_weight = jnp.where(suffix_allowed, jnp.exp(suffix_scores - row_max[..., None]), 0.0)
    total_weight = jnp.sum(prefix_weight, axis=-1) + jnp.sum(suffix_weight, axis=-1)
    weighted = jnp.einsum(
        "thep,phd->thed", prefix_weight.astype(jnp.bfloat16), cached[:, :, 1],
        preferred_element_type=jnp.float32,
    )
    weighted = weighted + jnp.einsum(
        "theu,uhd->thed", suffix_weight.astype(jnp.bfloat16), own_entries[:, :, 1],
        preferred_element_type=jnp.float32,
    )
    live_grid = live_slots[:, None, None]
    safe_total = jnp.where(live_grid, total_weight, 1.0)
    result = jnp.where(live_grid[..., None], weighted / safe_total[..., None], 0.0)
    return result.astype(jnp.bfloat16).reshape(token_rows, local_heads * 2 * HEAD)


def solution(mesh):
    sizes = tuple(s for _, s in SEQ_PARTS) + (mesh.shape["tp"],)
    names = tuple(n for n, _ in SEQ_PARTS) + ("tp",)
    fine = Mesh(mesh.devices.reshape(sizes), names)
    seq = names[:-1]
    in_specs = (P(seq, "tp"), P(seq, "tp"), P(seq + ("tp",), None), P(), P(seq), P(seq))
    out_specs = P(seq, "tp")
    return jax.shard_map(
        per_device, mesh=fine, in_specs=in_specs, out_specs=out_specs, check_vma=False
    )
```

```python
import math

import jax
import jax.numpy as jnp
import numpy as np
from jax import lax
from jax.sharding import Mesh
from jax.sharding import PartitionSpec as P

HEADS = 16
HEAD = 128

masked_score = -1e30

SEQ_PARTS = (("x", 4), ("zh", 2), ("y", 8), ("core", 2))


def spread(held, axes, count):
    outgoing = jnp.broadcast_to(held[None], (count,) + held.shape)
    return lax.all_to_all(outgoing, axes, split_axis=0, concat_axis=3, tiled=True)[0]


def gather_cache(prefix_cache, block_prefix, tensor_count, local_heads):
    block_rows = prefix_cache.shape[0]
    size = dict(SEQ_PARTS)
    local = prefix_cache.reshape(block_rows, tensor_count, local_heads, 2, HEAD).transpose(1, 3, 2, 0, 4)
    outgoing = jnp.broadcast_to(local[None], (size["zh"],) + local.shape)
    outgoing = outgoing.reshape((size["zh"] * tensor_count,) + local.shape[1:])
    mine = lax.all_to_all(outgoing, ("zh", "tp"), split_axis=0, concat_axis=3, tiled=True)[0]
    mine = spread(mine, ("y",), size["y"])
    mine = spread(mine, ("x",), size["x"])
    other = lax.ppermute(mine, "core", [(0, 1), (1, 0)])
    grid = block_prefix.reshape(size["x"], size["zh"], size["y"], size["core"], tensor_count)
    grid = grid.transpose(0, 2, 1, 3, 4)
    core = lax.axis_index("core")
    own_owner = jnp.repeat(jnp.take(grid, core, axis=3).reshape(-1), block_rows)
    other_owner = jnp.repeat(jnp.take(grid, 1 - core, axis=3).reshape(-1), block_rows)
    return (mine, own_owner), (other, other_owner)


def token_layout(lengths, prefixes, slots):
    cumulative = jnp.cumsum(lengths)
    slot_ids = jnp.arange(slots, dtype=jnp.int32)
    request_ids = jnp.sum((slot_ids[:, None] >= cumulative[None, :]).astype(jnp.int32), axis=1)
    live_slots = slot_ids < cumulative[-1]
    onehot = request_ids[:, None] == jnp.arange(lengths.shape[0], dtype=jnp.int32)[None, :]
    token_group = jnp.sum(jnp.where(onehot, prefixes[None, :], 0), axis=1)
    return (slot_ids, request_ids, live_slots, token_group)


def per_device(
    queries, suffix_entries, prefix_cache, block_prefix, request_lengths, request_prefix
):
    tensor_count = lax.axis_size("tp")
    local_heads = HEADS // tensor_count
    token_rows = queries.shape[0]
    block_rows = prefix_cache.shape[0]
    column_count = prefix_cache.shape[1] // tensor_count
    slot_ids, request_ids, live_slots, token_group = token_layout(
        request_lengths, request_prefix, token_rows
    )
    halves = gather_cache(prefix_cache, block_prefix, tensor_count, local_heads)

    query_rows = queries.reshape(token_rows, local_heads, 2, HEAD)
    own_entries = suffix_entries.reshape(token_rows, local_heads, 2, HEAD)
    scale = 1.0 / math.sqrt(HEAD)
    suffix_allowed = (
        (request_ids[:, None] == request_ids[None, :])
        & (slot_ids[None, :] <= slot_ids[:, None])
        & live_slots[:, None]
    )[:, None, None, :]
    suffix_scores = jnp.einsum(
        "thed,uhd->theu", query_rows, own_entries[:, :, 0], preferred_element_type=jnp.float32
    ) * scale
    suffix_scores = jnp.where(suffix_allowed, suffix_scores, masked_score)
    parts = []
    row_max = jnp.max(suffix_scores, axis=-1)
    for rows, owners in halves:
        allowed = ((token_group[:, None] == owners[None, :]) & live_slots[:, None])[:, None, None, :]
        scores = jnp.einsum(
            "thed,hpd->thep", query_rows, rows[0], preferred_element_type=jnp.float32
        ) * scale
        scores = jnp.where(allowed, scores, masked_score)
        row_max = jnp.maximum(row_max, jnp.max(scores, axis=-1))
        parts.append((scores, allowed, rows[1]))
    suffix_weight = jnp.where(suffix_allowed, jnp.exp(suffix_scores - row_max[..., None]), 0.0)
    total_weight = jnp.sum(suffix_weight, axis=-1)
    weighted = jnp.einsum(
        "theu,uhd->thed", suffix_weight.astype(jnp.bfloat16), own_entries[:, :, 1],
        preferred_element_type=jnp.float32,
    )
    for scores, allowed, values in parts:
        weight = jnp.where(allowed, jnp.exp(scores - row_max[..., None]), 0.0)
        total_weight = total_weight + jnp.sum(weight, axis=-1)
        weighted = weighted + jnp.einsum(
            "thep,hpd->thed", weight.astype(jnp.bfloat16), values,
            preferred_element_type=jnp.float32,
        )
    live_grid = live_slots[:, None, None]
    safe_total = jnp.where(live_grid, total_weight, 1.0)
    result = jnp.where(live_grid[..., None], weighted / safe_total[..., None], 0.0)
    return result.astype(jnp.bfloat16).reshape(token_rows, local_heads * 2 * HEAD)


def solution(mesh):
    sizes = tuple(s for _, s in SEQ_PARTS) + (mesh.shape["tp"],)
    names = tuple(n for n, _ in SEQ_PARTS) + ("tp",)
    fine = Mesh(mesh.devices.reshape(sizes), names)
    seq = names[:-1]
    in_specs = (P(seq, "tp"), P(seq, "tp"), P(seq + ("tp",), None), P(), P(seq), P(seq))
    out_specs = P(seq, "tp")
    return jax.shard_map(
        per_device, mesh=fine, in_specs=in_specs, out_specs=out_specs, check_vma=False
    )
```

```python
import math

import jax
import jax.numpy as jnp
import numpy as np
from jax import lax
from jax.sharding import Mesh
from jax.sharding import PartitionSpec as P

HEADS = 16
HEAD = 128

masked_score = -1e30

SEQ_PARTS = (("x", 4), ("zh", 2), ("y", 8), ("core", 2))


def spread(held, axes, count):
    outgoing = jnp.broadcast_to(held[None], (count,) + held.shape)
    return lax.all_to_all(outgoing, axes, split_axis=0, concat_axis=3, tiled=True)[0]


def gather_cache(prefix_cache, block_prefix, tensor_count, local_heads):
    block_rows = prefix_cache.shape[0]
    size = dict(SEQ_PARTS)
    local = prefix_cache.reshape(block_rows, tensor_count, local_heads, 2, HEAD).transpose(1, 3, 2, 0, 4)
    lines = size["y"] * size["zh"]
    outgoing = jnp.broadcast_to(local[None], (lines,) + local.shape)
    outgoing = outgoing.reshape((lines * tensor_count,) + local.shape[1:])
    mine = lax.all_to_all(outgoing, ("y", "zh", "tp"), split_axis=0, concat_axis=3, tiled=True)[0]
    mine = spread(mine, ("x",), size["x"])
    other = lax.ppermute(mine, "core", [(0, 1), (1, 0)])
    grid = block_prefix.reshape(size["x"], size["zh"], size["y"], size["core"], tensor_count)
    grid = grid.transpose(0, 2, 1, 3, 4)
    core = lax.axis_index("core")
    own_owner = jnp.repeat(jnp.take(grid, core, axis=3).reshape(-1), block_rows)
    other_owner = jnp.repeat(jnp.take(grid, 1 - core, axis=3).reshape(-1), block_rows)
    return (mine, own_owner), (other, other_owner)


def token_layout(lengths, prefixes, slots):
    cumulative = jnp.cumsum(lengths)
    slot_ids = jnp.arange(slots, dtype=jnp.int32)
    request_ids = jnp.sum((slot_ids[:, None] >= cumulative[None, :]).astype(jnp.int32), axis=1)
    live_slots = slot_ids < cumulative[-1]
    onehot = request_ids[:, None] == jnp.arange(lengths.shape[0], dtype=jnp.int32)[None, :]
    token_group = jnp.sum(jnp.where(onehot, prefixes[None, :], 0), axis=1)
    return (slot_ids, request_ids, live_slots, token_group)


def per_device(
    queries, suffix_entries, prefix_cache, block_prefix, request_lengths, request_prefix
):
    tensor_count = lax.axis_size("tp")
    local_heads = HEADS // tensor_count
    token_rows = queries.shape[0]
    block_rows = prefix_cache.shape[0]
    column_count = prefix_cache.shape[1] // tensor_count
    slot_ids, request_ids, live_slots, token_group = token_layout(
        request_lengths, request_prefix, token_rows
    )
    halves = gather_cache(prefix_cache, block_prefix, tensor_count, local_heads)

    query_rows = queries.reshape(token_rows, local_heads, 2, HEAD)
    own_entries = suffix_entries.reshape(token_rows, local_heads, 2, HEAD)
    scale = 1.0 / math.sqrt(HEAD)
    suffix_allowed = (
        (request_ids[:, None] == request_ids[None, :])
        & (slot_ids[None, :] <= slot_ids[:, None])
        & live_slots[:, None]
    )[:, None, None, :]
    suffix_scores = jnp.einsum(
        "thed,uhd->theu", query_rows, own_entries[:, :, 0], preferred_element_type=jnp.float32
    ) * scale
    suffix_scores = jnp.where(suffix_allowed, suffix_scores, masked_score)
    parts = []
    row_max = jnp.max(suffix_scores, axis=-1)
    for rows, owners in halves:
        allowed = ((token_group[:, None] == owners[None, :]) & live_slots[:, None])[:, None, None, :]
        scores = jnp.einsum(
            "thed,hpd->thep", query_rows, rows[0], preferred_element_type=jnp.float32
        ) * scale
        scores = jnp.where(allowed, scores, masked_score)
        row_max = jnp.maximum(row_max, jnp.max(scores, axis=-1))
        parts.append((scores, allowed, rows[1]))
    suffix_weight = jnp.where(suffix_allowed, jnp.exp(suffix_scores - row_max[..., None]), 0.0)
    total_weight = jnp.sum(suffix_weight, axis=-1)
    weighted = jnp.einsum(
        "theu,uhd->thed", suffix_weight.astype(jnp.bfloat16), own_entries[:, :, 1],
        preferred_element_type=jnp.float32,
    )
    for scores, allowed, values in parts:
        weight = jnp.where(allowed, jnp.exp(scores - row_max[..., None]), 0.0)
        total_weight = total_weight + jnp.sum(weight, axis=-1)
        weighted = weighted + jnp.einsum(
            "thep,hpd->thed", weight.astype(jnp.bfloat16), values,
            preferred_element_type=jnp.float32,
        )
    live_grid = live_slots[:, None, None]
    safe_total = jnp.where(live_grid, total_weight, 1.0)
    result = jnp.where(live_grid[..., None], weighted / safe_total[..., None], 0.0)
    return result.astype(jnp.bfloat16).reshape(token_rows, local_heads * 2 * HEAD)


def solution(mesh):
    sizes = tuple(s for _, s in SEQ_PARTS) + (mesh.shape["tp"],)
    names = tuple(n for n, _ in SEQ_PARTS) + ("tp",)
    fine = Mesh(mesh.devices.reshape(sizes), names)
    seq = names[:-1]
    in_specs = (P(seq, "tp"), P(seq, "tp"), P(seq + ("tp",), None), P(), P(seq), P(seq))
    out_specs = P(seq, "tp")
    return jax.shard_map(
        per_device, mesh=fine, in_specs=in_specs, out_specs=out_specs, check_vma=False
    )
```

```python
import math

import jax
import jax.numpy as jnp
import numpy as np
from jax import lax
from jax.sharding import Mesh
from jax.sharding import PartitionSpec as P

HEADS = 16
HEAD = 128

masked_score = -1e30

SEQ_PARTS = (("x", 4), ("zh", 2), ("y", 8), ("core", 2))


def spread(held, axes, count):
    outgoing = jnp.broadcast_to(held[None], (count,) + held.shape)
    return lax.all_to_all(outgoing, axes, split_axis=0, concat_axis=3, tiled=True)[0]


def gather_cache(prefix_cache, block_prefix, tensor_count, local_heads):
    block_rows = prefix_cache.shape[0]
    size = dict(SEQ_PARTS)
    local = prefix_cache.reshape(block_rows, tensor_count, local_heads, 2, HEAD).transpose(1, 3, 2, 0, 4)
    lines = size["y"] * size["zh"]
    outgoing = jnp.broadcast_to(local[None], (lines,) + local.shape)
    outgoing = outgoing.reshape((lines * tensor_count,) + local.shape[1:])
    mine = lax.all_to_all(outgoing, ("y", "zh", "tp"), split_axis=0, concat_axis=3, tiled=True)[0]
    rows = mine.shape[2]
    count = size["x"]
    here = lax.axis_index("x")
    core = lax.axis_index("core")
    swap = [(0, 1), (1, 0)]

    def shift(held, step):
        return lax.ppermute(held, "x", [(i, (i + step) % count) for i in range(count)])

    far = shift(mine[:, :, : rows // 2], 2)
    near = shift(mine[:, :, rows // 2 :], -2)
    pieces = [(mine, 0), (shift(mine, 1), -1), (shift(mine, -1), 1), (jnp.concatenate([far, near], axis=2), 2)]
    grid = block_prefix.reshape(size["x"], size["zh"], size["y"], size["core"], tensor_count)
    grid = grid.transpose(0, 2, 1, 3, 4)
    blocks = []
    for held, offset in pieces:
        source = (here + offset) % count
        line = jnp.take(grid, source, axis=0)
        own_owner = jnp.repeat(jnp.take(line, core, axis=2).reshape(-1), block_rows)
        other_owner = jnp.repeat(jnp.take(line, 1 - core, axis=2).reshape(-1), block_rows)
        blocks.append((held, own_owner))
        blocks.append((lax.ppermute(held, "core", swap), other_owner))
    return blocks


def token_layout(lengths, prefixes, slots):
    cumulative = jnp.cumsum(lengths)
    slot_ids = jnp.arange(slots, dtype=jnp.int32)
    request_ids = jnp.sum((slot_ids[:, None] >= cumulative[None, :]).astype(jnp.int32), axis=1)
    live_slots = slot_ids < cumulative[-1]
    onehot = request_ids[:, None] == jnp.arange(lengths.shape[0], dtype=jnp.int32)[None, :]
    token_group = jnp.sum(jnp.where(onehot, prefixes[None, :], 0), axis=1)
    return (slot_ids, request_ids, live_slots, token_group)


def per_device(
    queries, suffix_entries, prefix_cache, block_prefix, request_lengths, request_prefix
):
    tensor_count = lax.axis_size("tp")
    local_heads = HEADS // tensor_count
    token_rows = queries.shape[0]
    block_rows = prefix_cache.shape[0]
    column_count = prefix_cache.shape[1] // tensor_count
    slot_ids, request_ids, live_slots, token_group = token_layout(
        request_lengths, request_prefix, token_rows
    )
    halves = gather_cache(prefix_cache, block_prefix, tensor_count, local_heads)

    query_rows = queries.reshape(token_rows, local_heads, 2, HEAD)
    own_entries = suffix_entries.reshape(token_rows, local_heads, 2, HEAD)
    scale = 1.0 / math.sqrt(HEAD)
    suffix_allowed = (
        (request_ids[:, None] == request_ids[None, :])
        & (slot_ids[None, :] <= slot_ids[:, None])
        & live_slots[:, None]
    )[:, None, None, :]
    suffix_scores = jnp.einsum(
        "thed,uhd->theu", query_rows, own_entries[:, :, 0], preferred_element_type=jnp.float32
    ) * scale
    suffix_scores = jnp.where(suffix_allowed, suffix_scores, masked_score)
    parts = []
    row_max = jnp.max(suffix_scores, axis=-1)
    for rows, owners in halves:
        allowed = ((token_group[:, None] == owners[None, :]) & live_slots[:, None])[:, None, None, :]
        scores = jnp.einsum(
            "thed,hpd->thep", query_rows, rows[0], preferred_element_type=jnp.float32
        ) * scale
        scores = jnp.where(allowed, scores, masked_score)
        row_max = jnp.maximum(row_max, jnp.max(scores, axis=-1))
        parts.append((scores, allowed, rows[1]))
    suffix_weight = jnp.where(suffix_allowed, jnp.exp(suffix_scores - row_max[..., None]), 0.0)
    total_weight = jnp.sum(suffix_weight, axis=-1)
    weighted = jnp.einsum(
        "theu,uhd->thed", suffix_weight.astype(jnp.bfloat16), own_entries[:, :, 1],
        preferred_element_type=jnp.float32,
    )
    for scores, allowed, values in parts:
        weight = jnp.where(allowed, jnp.exp(scores - row_max[..., None]), 0.0)
        total_weight = total_weight + jnp.sum(weight, axis=-1)
        weighted = weighted + jnp.einsum(
            "thep,hpd->thed", weight.astype(jnp.bfloat16), values,
            preferred_element_type=jnp.float32,
        )
    live_grid = live_slots[:, None, None]
    safe_total = jnp.where(live_grid, total_weight, 1.0)
    result = jnp.where(live_grid[..., None], weighted / safe_total[..., None], 0.0)
    return result.astype(jnp.bfloat16).reshape(token_rows, local_heads * 2 * HEAD)


def solution(mesh):
    sizes = tuple(s for _, s in SEQ_PARTS) + (mesh.shape["tp"],)
    names = tuple(n for n, _ in SEQ_PARTS) + ("tp",)
    fine = Mesh(mesh.devices.reshape(sizes), names)
    seq = names[:-1]
    in_specs = (P(seq, "tp"), P(seq, "tp"), P(seq + ("tp",), None), P(), P(seq), P(seq))
    out_specs = P(seq, "tp")
    return jax.shard_map(
        per_device, mesh=fine, in_specs=in_specs, out_specs=out_specs, check_vma=False
    )
```

```python
import math

import jax
import jax.numpy as jnp
import numpy as np
from jax import lax
from jax.sharding import Mesh
from jax.sharding import PartitionSpec as P

HEADS = 16
HEAD = 128

masked_score = -1e30

SEQ_PARTS = (("x", 4), ("zh", 2), ("y", 8), ("core", 2))


def spread(held, axes, count):
    outgoing = jnp.broadcast_to(held[None], (count,) + held.shape)
    return lax.all_to_all(outgoing, axes, split_axis=0, concat_axis=3, tiled=True)[0]


def gather_cache(prefix_cache, block_prefix, tensor_count, local_heads):
    block_rows = prefix_cache.shape[0]
    size = dict(SEQ_PARTS)
    local = prefix_cache.reshape(block_rows, tensor_count, local_heads, 2, HEAD).transpose(1, 3, 2, 0, 4)
    lines = size["y"] * size["zh"]
    outgoing = jnp.broadcast_to(local[None], (lines,) + local.shape)
    outgoing = outgoing.reshape((lines * tensor_count,) + local.shape[1:])
    mine = lax.all_to_all(outgoing, ("y", "zh", "tp"), split_axis=0, concat_axis=3, tiled=True)[0]
    count = size["x"]
    here = lax.axis_index("x")
    core = lax.axis_index("core")
    swap = [(0, 1), (1, 0)]

    def shift(held, step):
        return lax.ppermute(held, "x", [(i, (i + step) % count) for i in range(count)])

    arrived = [(shift(mine, step), -step) for step in (1, -1, 2)]
    grid = block_prefix.reshape(size["x"], size["zh"], size["y"], size["core"], tensor_count)
    grid = grid.transpose(0, 2, 1, 3, 4)

    def owner_of(offset, which):
        line = jnp.take(grid, (here + offset) % count, axis=0)
        return jnp.repeat(jnp.take(line, which, axis=2).reshape(-1), block_rows)

    blocks = [(mine, owner_of(0, core)), (lax.ppermute(mine, "core", swap), owner_of(0, 1 - core))]
    blocks += [(held, owner_of(offset, core)) for held, offset in arrived]
    forwarded = lax.ppermute(jnp.concatenate([held for held, _ in arrived], axis=2), "core", swap)
    blocks.append((forwarded, jnp.concatenate([owner_of(offset, 1 - core) for _, offset in arrived])))
    return blocks


def token_layout(lengths, prefixes, slots):
    cumulative = jnp.cumsum(lengths)
    slot_ids = jnp.arange(slots, dtype=jnp.int32)
    request_ids = jnp.sum((slot_ids[:, None] >= cumulative[None, :]).astype(jnp.int32), axis=1)
    live_slots = slot_ids < cumulative[-1]
    onehot = request_ids[:, None] == jnp.arange(lengths.shape[0], dtype=jnp.int32)[None, :]
    token_group = jnp.sum(jnp.where(onehot, prefixes[None, :], 0), axis=1)
    return (slot_ids, request_ids, live_slots, token_group)


def per_device(
    queries, suffix_entries, prefix_cache, block_prefix, request_lengths, request_prefix
):
    tensor_count = lax.axis_size("tp")
    local_heads = HEADS // tensor_count
    token_rows = queries.shape[0]
    block_rows = prefix_cache.shape[0]
    column_count = prefix_cache.shape[1] // tensor_count
    slot_ids, request_ids, live_slots, token_group = token_layout(
        request_lengths, request_prefix, token_rows
    )
    halves = gather_cache(prefix_cache, block_prefix, tensor_count, local_heads)

    query_rows = queries.reshape(token_rows, local_heads, 2, HEAD)
    own_entries = suffix_entries.reshape(token_rows, local_heads, 2, HEAD)
    scale = 1.0 / math.sqrt(HEAD)
    suffix_allowed = (
        (request_ids[:, None] == request_ids[None, :])
        & (slot_ids[None, :] <= slot_ids[:, None])
        & live_slots[:, None]
    )[:, None, None, :]
    suffix_scores = jnp.einsum(
        "thed,uhd->theu", query_rows, own_entries[:, :, 0], preferred_element_type=jnp.float32
    ) * scale
    suffix_scores = jnp.where(suffix_allowed, suffix_scores, masked_score)
    parts = []
    row_max = jnp.max(suffix_scores, axis=-1)
    for rows, owners in halves:
        allowed = ((token_group[:, None] == owners[None, :]) & live_slots[:, None])[:, None, None, :]
        scores = jnp.einsum(
            "thed,hpd->thep", query_rows, rows[0], preferred_element_type=jnp.float32
        ) * scale
        scores = jnp.where(allowed, scores, masked_score)
        row_max = jnp.maximum(row_max, jnp.max(scores, axis=-1))
        parts.append((scores, allowed, rows[1]))
    suffix_weight = jnp.where(suffix_allowed, jnp.exp(suffix_scores - row_max[..., None]), 0.0)
    total_weight = jnp.sum(suffix_weight, axis=-1)
    weighted = jnp.einsum(
        "theu,uhd->thed", suffix_weight.astype(jnp.bfloat16), own_entries[:, :, 1],
        preferred_element_type=jnp.float32,
    )
    for scores, allowed, values in parts:
        weight = jnp.where(allowed, jnp.exp(scores - row_max[..., None]), 0.0)
        total_weight = total_weight + jnp.sum(weight, axis=-1)
        weighted = weighted + jnp.einsum(
            "thep,hpd->thed", weight.astype(jnp.bfloat16), values,
            preferred_element_type=jnp.float32,
        )
    live_grid = live_slots[:, None, None]
    safe_total = jnp.where(live_grid, total_weight, 1.0)
    result = jnp.where(live_grid[..., None], weighted / safe_total[..., None], 0.0)
    return result.astype(jnp.bfloat16).reshape(token_rows, local_heads * 2 * HEAD)


def solution(mesh):
    sizes = tuple(s for _, s in SEQ_PARTS) + (mesh.shape["tp"],)
    names = tuple(n for n, _ in SEQ_PARTS) + ("tp",)
    fine = Mesh(mesh.devices.reshape(sizes), names)
    seq = names[:-1]
    in_specs = (P(seq, "tp"), P(seq, "tp"), P(seq + ("tp",), None), P(), P(seq), P(seq))
    out_specs = P(seq, "tp")
    return jax.shard_map(
        per_device, mesh=fine, in_specs=in_specs, out_specs=out_specs, check_vma=False
    )
```

```python
import math

import jax
import jax.numpy as jnp
from jax import lax
from jax.sharding import Mesh
from jax.sharding import PartitionSpec as P


HEADS = 16
HEAD = 128

masked_score = -1e30

SEQ_PARTS = (("x", 4), ("zh", 2), ("y", 8), ("core", 2))


def gather_cache(prefix_cache, block_prefix, tensor_count, local_heads):
    block_rows = prefix_cache.shape[0]
    size = dict(SEQ_PARTS)
    local = prefix_cache.reshape(block_rows, tensor_count, local_heads, 2, HEAD).transpose(1, 3, 2, 0, 4)
    lines = size["y"] * size["zh"]
    outgoing = jnp.broadcast_to(local[None], (lines,) + local.shape)
    outgoing = outgoing.reshape((lines * tensor_count,) + local.shape[1:])
    mine = lax.all_to_all(outgoing, ("y", "zh", "tp"), split_axis=0, concat_axis=3, tiled=True)[0]
    count = size["x"]
    here = lax.axis_index("x")
    core = lax.axis_index("core")
    swap = [(0, 1), (1, 0)]

    def shift(held, step):
        return lax.ppermute(held, "x", [(i, (i + step) % count) for i in range(count)])

    partner = lax.ppermute(mine, "core", swap)
    arrived = [(shift(mine, step), -step) for step in (1, -1, 2)]
    grid = block_prefix.reshape(size["x"], size["zh"], size["y"], size["core"], tensor_count)
    grid = grid.transpose(0, 2, 1, 3, 4)

    def owner_of(offset, which):
        line = jnp.take(grid, (here + offset) % count, axis=0)
        return jnp.repeat(jnp.take(line, which, axis=2).reshape(-1), block_rows)

    blocks = [(mine, owner_of(0, core)), (partner, owner_of(0, 1 - core))]
    blocks += [(held, owner_of(offset, core)) for held, offset in arrived]
    forwarded = lax.ppermute(jnp.concatenate([held for held, _ in arrived], axis=2), "core", swap)
    blocks.append((forwarded, jnp.concatenate([owner_of(offset, 1 - core) for _, offset in arrived])))
    return blocks


def token_layout(lengths, prefixes, slots):
    cumulative = jnp.cumsum(lengths)
    slot_ids = jnp.arange(slots, dtype=jnp.int32)
    request_ids = jnp.sum((slot_ids[:, None] >= cumulative[None, :]).astype(jnp.int32), axis=1)
    live_slots = slot_ids < cumulative[-1]
    onehot = request_ids[:, None] == jnp.arange(lengths.shape[0], dtype=jnp.int32)[None, :]
    token_group = jnp.sum(jnp.where(onehot, prefixes[None, :], 0), axis=1)
    return (slot_ids, request_ids, live_slots, token_group)


def per_device(
    queries, suffix_entries, prefix_cache, block_prefix, request_lengths, request_prefix
):
    tensor_count = lax.axis_size("tp")
    local_heads = HEADS // tensor_count
    token_rows = queries.shape[0]
    slot_ids, request_ids, live_slots, token_group = token_layout(
        request_lengths, request_prefix, token_rows
    )
    halves = gather_cache(prefix_cache, block_prefix, tensor_count, local_heads)

    query_rows = queries.reshape(token_rows, local_heads, 2, HEAD)
    own_entries = suffix_entries.reshape(token_rows, local_heads, 2, HEAD)
    scale = 1.0 / math.sqrt(HEAD)
    suffix_allowed = (
        (request_ids[:, None] == request_ids[None, :])
        & (slot_ids[None, :] <= slot_ids[:, None])
        & live_slots[:, None]
    )[:, None, None, :]
    suffix_scores = jnp.einsum(
        "thed,uhd->theu", query_rows, own_entries[:, :, 0], preferred_element_type=jnp.float32
    ) * scale
    suffix_scores = jnp.where(suffix_allowed, suffix_scores, masked_score)
    parts = []
    row_max = jnp.max(suffix_scores, axis=-1)
    for rows, owners in halves:
        allowed = ((token_group[:, None] == owners[None, :]) & live_slots[:, None])[:, None, None, :]
        scores = jnp.einsum(
            "thed,hpd->thep", query_rows, rows[0], preferred_element_type=jnp.float32
        ) * scale
        scores = jnp.where(allowed, scores, masked_score)
        row_max = jnp.maximum(row_max, jnp.max(scores, axis=-1))
        parts.append((scores, allowed, rows[1]))
    suffix_weight = jnp.where(suffix_allowed, jnp.exp(suffix_scores - row_max[..., None]), 0.0)
    total_weight = jnp.sum(suffix_weight, axis=-1)
    weighted = jnp.einsum(
        "theu,uhd->thed", suffix_weight.astype(jnp.bfloat16), own_entries[:, :, 1],
        preferred_element_type=jnp.float32,
    )
    for scores, allowed, values in parts:
        weight = jnp.where(allowed, jnp.exp(scores - row_max[..., None]), 0.0)
        total_weight = total_weight + jnp.sum(weight, axis=-1)
        weighted = weighted + jnp.einsum(
            "thep,hpd->thed", weight.astype(jnp.bfloat16), values,
            preferred_element_type=jnp.float32,
        )
    live_grid = live_slots[:, None, None]
    safe_total = jnp.where(live_grid, total_weight, 1.0)
    result = jnp.where(live_grid[..., None], weighted / safe_total[..., None], 0.0)
    return result.astype(jnp.bfloat16).reshape(token_rows, local_heads * 2 * HEAD)


def solution(mesh):
    sizes = tuple(s for _, s in SEQ_PARTS) + (mesh.shape["tp"],)
    names = tuple(n for n, _ in SEQ_PARTS) + ("tp",)
    fine = Mesh(mesh.devices.reshape(sizes), names)
    seq = names[:-1]
    in_specs = (P(seq, "tp"), P(seq, "tp"), P(seq + ("tp",), None), P(), P(seq), P(seq))
    out_specs = P(seq, "tp")
    return jax.shard_map(per_device, mesh=fine, in_specs=in_specs, out_specs=out_specs, check_vma=False)
```

```python
import math

import jax
import jax.numpy as jnp
import numpy as np
from jax import lax
from jax.sharding import Mesh
from jax.sharding import PartitionSpec as P

HEADS = 16
HEAD = 128

masked_score = -1e30

SEQ_PARTS = (("x", 4), ("zh", 2), ("y", 8), ("core", 2))


def spread(held, axes, count):
    outgoing = jnp.broadcast_to(held[None], (count,) + held.shape)
    return lax.all_to_all(outgoing, axes, split_axis=0, concat_axis=3, tiled=True)[0]


def gather_cache(prefix_cache, block_prefix, tensor_count, local_heads):
    block_rows = prefix_cache.shape[0]
    size = dict(SEQ_PARTS)
    local = prefix_cache.reshape(block_rows, tensor_count, local_heads, 2, HEAD).transpose(1, 3, 2, 0, 4)
    lines = size["y"] * size["zh"]
    outgoing = jnp.broadcast_to(local[None], (lines,) + local.shape)
    outgoing = outgoing.reshape((lines * tensor_count,) + local.shape[1:])
    mine = lax.all_to_all(outgoing, ("y", "zh", "tp"), split_axis=0, concat_axis=3, tiled=True)[0]
    count = size["x"]
    here = lax.axis_index("x")
    core = lax.axis_index("core")
    swap = [(0, 1), (1, 0)]

    def shift(held, step):
        return lax.ppermute(held, "x", [(i, (i + step) % count) for i in range(count)])

    arrived = [(shift(mine, step), -step) for step in (1, -1, 2)]
    grid = block_prefix.reshape(size["x"], size["zh"], size["y"], size["core"], tensor_count)
    grid = grid.transpose(0, 2, 1, 3, 4)

    def owner_of(offset, which):
        line = jnp.take(grid, (here + offset) % count, axis=0)
        return jnp.repeat(jnp.take(line, which, axis=2).reshape(-1), block_rows)

    blocks = [(mine, owner_of(0, core)), (lax.ppermute(mine, "core", swap), owner_of(0, 1 - core))]
    blocks += [(held, owner_of(offset, core)) for held, offset in arrived]
    forwarded = lax.ppermute(jnp.concatenate([held for held, _ in arrived], axis=2), "core", swap)
    blocks.append((forwarded, jnp.concatenate([owner_of(offset, 1 - core) for _, offset in arrived])))
    return blocks


def fold_block(running, query_rows, keys, values, allowed):
    scores = jnp.einsum("thed,hpd->thep", query_rows, keys, preferred_element_type=jnp.float32)
    scores = jnp.where(allowed, scores * (1.0 / math.sqrt(HEAD)), masked_score)
    block_max = jnp.max(scores, axis=-1)
    if running is None:
        new_max = block_max
    else:
        old_max, old_total, old_sum = running
        new_max = jnp.maximum(old_max, block_max)
    weights = jnp.where(allowed, jnp.exp(scores - new_max[..., None]), 0.0)
    products = jnp.einsum(
        "thep,hpd->thed", weights.astype(jnp.bfloat16), values, preferred_element_type=jnp.float32
    )
    total = jnp.sum(weights, axis=-1)
    if running is not None:
        rescale = jnp.exp(old_max - new_max)
        total = old_total * rescale + total
        products = old_sum * rescale[..., None] + products
    return new_max, total, products


def token_layout(lengths, prefixes, slots):
    cumulative = jnp.cumsum(lengths)
    slot_ids = jnp.arange(slots, dtype=jnp.int32)
    request_ids = jnp.sum((slot_ids[:, None] >= cumulative[None, :]).astype(jnp.int32), axis=1)
    live_slots = slot_ids < cumulative[-1]
    onehot = request_ids[:, None] == jnp.arange(lengths.shape[0], dtype=jnp.int32)[None, :]
    token_group = jnp.sum(jnp.where(onehot, prefixes[None, :], 0), axis=1)
    return (slot_ids, request_ids, live_slots, token_group)


def per_device(
    queries, suffix_entries, prefix_cache, block_prefix, request_lengths, request_prefix
):
    tensor_count = lax.axis_size("tp")
    local_heads = HEADS // tensor_count
    token_rows = queries.shape[0]
    block_rows = prefix_cache.shape[0]
    column_count = prefix_cache.shape[1] // tensor_count
    slot_ids, request_ids, live_slots, token_group = token_layout(
        request_lengths, request_prefix, token_rows
    )
    halves = gather_cache(prefix_cache, block_prefix, tensor_count, local_heads)

    query_rows = queries.reshape(token_rows, local_heads, 2, HEAD)
    own_entries = suffix_entries.reshape(token_rows, local_heads, 2, HEAD)
    suffix_allowed = (
        (request_ids[:, None] == request_ids[None, :])
        & (slot_ids[None, :] <= slot_ids[:, None])
        & live_slots[:, None]
    )[:, None, None, :]
    own_keys = own_entries[:, :, 0].transpose(1, 0, 2)
    own_values = own_entries[:, :, 1].transpose(1, 0, 2)
    running = fold_block(None, query_rows, own_keys, own_values, suffix_allowed)
    for rows, owners in halves:
        allowed = ((token_group[:, None] == owners[None, :]) & live_slots[:, None])[:, None, None, :]
        running = fold_block(running, query_rows, rows[0], rows[1], allowed)
    row_max, total_weight, weighted = running
    live_grid = live_slots[:, None, None]
    safe_total = jnp.where(live_grid, total_weight, 1.0)
    result = jnp.where(live_grid[..., None], weighted / safe_total[..., None], 0.0)
    return result.astype(jnp.bfloat16).reshape(token_rows, local_heads * 2 * HEAD)


def solution(mesh):
    sizes = tuple(s for _, s in SEQ_PARTS) + (mesh.shape["tp"],)
    names = tuple(n for n, _ in SEQ_PARTS) + ("tp",)
    fine = Mesh(mesh.devices.reshape(sizes), names)
    seq = names[:-1]
    in_specs = (P(seq, "tp"), P(seq, "tp"), P(seq + ("tp",), None), P(), P(seq), P(seq))
    out_specs = P(seq, "tp")
    return jax.shard_map(
        per_device, mesh=fine, in_specs=in_specs, out_specs=out_specs, check_vma=False
    )
```

```python
import math

import jax
import jax.numpy as jnp
from jax import lax
from jax.sharding import Mesh
from jax.sharding import PartitionSpec as P


HEADS = 16
HEAD = 128

masked_score = -1e30

SEQ_PARTS = (("x", 4), ("zh", 2), ("y", 8), ("core", 2))


def gather_cache(prefix_cache, block_prefix, tensor_count, local_heads):
    block_rows = prefix_cache.shape[0]
    size = dict(SEQ_PARTS)
    local = prefix_cache.reshape(block_rows, tensor_count, local_heads, 2, HEAD).transpose(1, 3, 2, 0, 4)
    lines = size["y"] * size["zh"]
    outgoing = jnp.broadcast_to(local[None], (lines,) + local.shape)
    outgoing = outgoing.reshape((lines * tensor_count,) + local.shape[1:])
    mine = lax.all_to_all(outgoing, ("y", "zh", "tp"), split_axis=0, concat_axis=3, tiled=True)[0]
    count = size["x"]
    here = lax.axis_index("x")
    core = lax.axis_index("core")
    swap = [(0, 1), (1, 0)]

    def shift(held, step):
        return lax.ppermute(held, "x", [(i, (i + step) % count) for i in range(count)])

    arrived = [(shift(mine, step), -step) for step in (1, -1, 2)]
    grid = block_prefix.reshape(size["x"], size["zh"], size["y"], size["core"], tensor_count)
    grid = grid.transpose(0, 2, 1, 3, 4)

    def owner_of(offset, which):
        line = jnp.take(grid, (here + offset) % count, axis=0)
        return jnp.repeat(jnp.take(line, which, axis=2).reshape(-1), block_rows)

    blocks = [(mine, owner_of(0, core)), (lax.ppermute(mine, "core", swap), owner_of(0, 1 - core))]
    blocks += [(held, owner_of(offset, core)) for held, offset in arrived]
    forwarded = lax.ppermute(jnp.concatenate([held for held, _ in arrived], axis=2), "core", swap)
    blocks.append((forwarded, jnp.concatenate([owner_of(offset, 1 - core) for _, offset in arrived])))
    return blocks


def fold_block(running, query_rows, keys, values, allowed):
    scores = jnp.einsum("thed,hpd->thep", query_rows, keys, preferred_element_type=jnp.float32)
    scores = jnp.where(allowed, scores * (1.0 / math.sqrt(HEAD)), masked_score)
    block_max = jnp.max(scores, axis=-1)
    if running is None:
        new_max = block_max
    else:
        old_max, old_total, old_sum = running
        new_max = jnp.maximum(old_max, block_max)
    weights = jnp.where(allowed, jnp.exp(scores - new_max[..., None]), 0.0)
    products = jnp.einsum(
        "thep,hpd->thed", weights.astype(jnp.bfloat16), values, preferred_element_type=jnp.float32
    )
    total = jnp.sum(weights, axis=-1)
    if running is not None:
        rescale = jnp.exp(old_max - new_max)
        total = old_total * rescale + total
        products = old_sum * rescale[..., None] + products
    return new_max, total, products


def token_layout(lengths, prefixes, slots):
    cumulative = jnp.cumsum(lengths)
    slot_ids = jnp.arange(slots, dtype=jnp.int32)
    request_ids = jnp.sum((slot_ids[:, None] >= cumulative[None, :]).astype(jnp.int32), axis=1)
    live_slots = slot_ids < cumulative[-1]
    onehot = request_ids[:, None] == jnp.arange(lengths.shape[0], dtype=jnp.int32)[None, :]
    token_group = jnp.sum(jnp.where(onehot, prefixes[None, :], 0), axis=1)
    return (slot_ids, request_ids, live_slots, token_group)


def per_device(
    queries, suffix_entries, prefix_cache, block_prefix, request_lengths, request_prefix
):
    tensor_count = lax.axis_size("tp")
    local_heads = HEADS // tensor_count
    token_rows = queries.shape[0]
    slot_ids, request_ids, live_slots, token_group = token_layout(
        request_lengths, request_prefix, token_rows
    )
    halves = gather_cache(prefix_cache, block_prefix, tensor_count, local_heads)

    query_rows = queries.reshape(token_rows, local_heads, 2, HEAD)
    own_entries = suffix_entries.reshape(token_rows, local_heads, 2, HEAD)
    suffix_allowed = (
        (request_ids[:, None] == request_ids[None, :])
        & (slot_ids[None, :] <= slot_ids[:, None])
        & live_slots[:, None]
    )[:, None, None, :]
    own_keys = own_entries[:, :, 0].transpose(1, 0, 2)
    own_values = own_entries[:, :, 1].transpose(1, 0, 2)
    running = fold_block(None, query_rows, own_keys, own_values, suffix_allowed)
    for rows, owners in halves:
        allowed = ((token_group[:, None] == owners[None, :]) & live_slots[:, None])[:, None, None, :]
        running = fold_block(running, query_rows, rows[0], rows[1], allowed)
    _, total_weight, weighted = running
    live_grid = live_slots[:, None, None]
    safe_total = jnp.where(live_grid, total_weight, 1.0)
    result = jnp.where(live_grid[..., None], weighted / safe_total[..., None], 0.0)
    return result.astype(jnp.bfloat16).reshape(token_rows, local_heads * 2 * HEAD)


def solution(mesh):
    sizes = tuple(s for _, s in SEQ_PARTS) + (mesh.shape["tp"],)
    names = tuple(n for n, _ in SEQ_PARTS) + ("tp",)
    fine = Mesh(mesh.devices.reshape(sizes), names)
    seq = names[:-1]
    in_specs = (P(seq, "tp"), P(seq, "tp"), P(seq + ("tp",), None), P(), P(seq), P(seq))
    out_specs = P(seq, "tp")
    return jax.shard_map(per_device, mesh=fine, in_specs=in_specs, out_specs=out_specs, check_vma=False)
```

```python
import math

import jax
import jax.numpy as jnp
import numpy as np
from jax import lax
from jax.sharding import Mesh
from jax.sharding import PartitionSpec as P

HEADS = 16
HEAD = 128

masked_score = -1e30

SEQ_PARTS = (("x", 4), ("zh", 2), ("y", 8), ("core", 2))


def spread(held, axes, count):
    outgoing = jnp.broadcast_to(held[None], (count,) + held.shape)
    return lax.all_to_all(outgoing, axes, split_axis=0, concat_axis=3, tiled=True)[0]


def gather_cache(prefix_cache, block_prefix, tensor_count, local_heads):
    block_rows = prefix_cache.shape[0]
    size = dict(SEQ_PARTS)
    local = prefix_cache.reshape(block_rows, tensor_count, local_heads, 2, HEAD).transpose(1, 3, 2, 0, 4)
    lines = size["y"] * size["zh"]
    outgoing = jnp.broadcast_to(local[None], (lines,) + local.shape)
    outgoing = outgoing.reshape((lines * tensor_count,) + local.shape[1:])
    mine = lax.all_to_all(outgoing, ("y", "zh", "tp"), split_axis=0, concat_axis=3, tiled=True)[0]
    count = size["x"]
    here = lax.axis_index("x")
    core = lax.axis_index("core")
    swap = [(0, 1), (1, 0)]

    def shift(held, step):
        return lax.ppermute(held, "x", [(i, (i + step) % count) for i in range(count)])

    arrived = [(shift(mine, step), -step) for step in (1, -1, 2)]
    grid = block_prefix.reshape(size["x"], size["zh"], size["y"], size["core"], tensor_count)
    grid = grid.transpose(0, 2, 1, 3, 4)

    def owner_of(offset, which):
        line = jnp.take(grid, (here + offset) % count, axis=0)
        return jnp.repeat(jnp.take(line, which, axis=2).reshape(-1), block_rows)

    blocks = [(mine, owner_of(0, core))]
    blocks += [(held, owner_of(offset, core)) for held, offset in arrived]
    everything = [(mine, 0)] + arrived
    forwarded = lax.ppermute(jnp.concatenate([held for held, _ in everything], axis=2), "core", swap)
    blocks.append((forwarded, jnp.concatenate([owner_of(offset, 1 - core) for _, offset in everything])))
    return blocks


def fold_block(running, query_rows, keys, values, allowed):
    scores = jnp.einsum("thed,hpd->thep", query_rows, keys, preferred_element_type=jnp.float32)
    scores = jnp.where(allowed, scores * (1.0 / math.sqrt(HEAD)), masked_score)
    block_max = jnp.max(scores, axis=-1)
    if running is None:
        new_max = block_max
    else:
        old_max, old_total, old_sum = running
        new_max = jnp.maximum(old_max, block_max)
    weights = jnp.where(allowed, jnp.exp(scores - new_max[..., None]), 0.0)
    products = jnp.einsum(
        "thep,hpd->thed", weights.astype(jnp.bfloat16), values, preferred_element_type=jnp.float32
    )
    total = jnp.sum(weights, axis=-1)
    if running is not None:
        rescale = jnp.exp(old_max - new_max)
        total = old_total * rescale + total
        products = old_sum * rescale[..., None] + products
    return new_max, total, products


def token_layout(lengths, prefixes, slots):
    cumulative = jnp.cumsum(lengths)
    slot_ids = jnp.arange(slots, dtype=jnp.int32)
    request_ids = jnp.sum((slot_ids[:, None] >= cumulative[None, :]).astype(jnp.int32), axis=1)
    live_slots = slot_ids < cumulative[-1]
    onehot = request_ids[:, None] == jnp.arange(lengths.shape[0], dtype=jnp.int32)[None, :]
    token_group = jnp.sum(jnp.where(onehot, prefixes[None, :], 0), axis=1)
    return (slot_ids, request_ids, live_slots, token_group)


def per_device(
    queries, suffix_entries, prefix_cache, block_prefix, request_lengths, request_prefix
):
    tensor_count = lax.axis_size("tp")
    local_heads = HEADS // tensor_count
    token_rows = queries.shape[0]
    block_rows = prefix_cache.shape[0]
    column_count = prefix_cache.shape[1] // tensor_count
    slot_ids, request_ids, live_slots, token_group = token_layout(
        request_lengths, request_prefix, token_rows
    )
    halves = gather_cache(prefix_cache, block_prefix, tensor_count, local_heads)

    query_rows = queries.reshape(token_rows, local_heads, 2, HEAD)
    own_entries = suffix_entries.reshape(token_rows, local_heads, 2, HEAD)
    suffix_allowed = (
        (request_ids[:, None] == request_ids[None, :])
        & (slot_ids[None, :] <= slot_ids[:, None])
        & live_slots[:, None]
    )[:, None, None, :]
    own_keys = own_entries[:, :, 0].transpose(1, 0, 2)
    own_values = own_entries[:, :, 1].transpose(1, 0, 2)
    running = fold_block(None, query_rows, own_keys, own_values, suffix_allowed)
    for rows, owners in halves:
        allowed = ((token_group[:, None] == owners[None, :]) & live_slots[:, None])[:, None, None, :]
        running = fold_block(running, query_rows, rows[0], rows[1], allowed)
    row_max, total_weight, weighted = running
    live_grid = live_slots[:, None, None]
    safe_total = jnp.where(live_grid, total_weight, 1.0)
    result = jnp.where(live_grid[..., None], weighted / safe_total[..., None], 0.0)
    return result.astype(jnp.bfloat16).reshape(token_rows, local_heads * 2 * HEAD)


def solution(mesh):
    sizes = tuple(s for _, s in SEQ_PARTS) + (mesh.shape["tp"],)
    names = tuple(n for n, _ in SEQ_PARTS) + ("tp",)
    fine = Mesh(mesh.devices.reshape(sizes), names)
    seq = names[:-1]
    in_specs = (P(seq, "tp"), P(seq, "tp"), P(seq + ("tp",), None), P(), P(seq), P(seq))
    out_specs = P(seq, "tp")
    return jax.shard_map(
        per_device, mesh=fine, in_specs=in_specs, out_specs=out_specs, check_vma=False
    )
```

```python
import math

import jax
import jax.numpy as jnp
import numpy as np
from jax import lax
from jax.sharding import Mesh
from jax.sharding import PartitionSpec as P

HEADS = 16
HEAD = 128

masked_score = -1e30

SEQ_PARTS = (("x", 4), ("zh", 2), ("y", 8), ("core", 2))


def spread(held, axes, count):
    outgoing = jnp.broadcast_to(held[None], (count,) + held.shape)
    return lax.all_to_all(outgoing, axes, split_axis=0, concat_axis=3, tiled=True)[0]


def gather_cache(prefix_cache, block_prefix, tensor_count, local_heads):
    block_rows = prefix_cache.shape[0]
    size = dict(SEQ_PARTS)
    local = prefix_cache.reshape(block_rows, tensor_count, local_heads, 2, HEAD).transpose(1, 3, 2, 0, 4)
    lines = size["y"] * size["zh"]
    outgoing = jnp.broadcast_to(local[None], (lines,) + local.shape)
    outgoing = outgoing.reshape((lines * tensor_count,) + local.shape[1:])
    mine = lax.all_to_all(outgoing, ("y", "zh", "tp"), split_axis=0, concat_axis=3, tiled=True)[0]
    count = size["x"]
    here = lax.axis_index("x")
    core = lax.axis_index("core")
    swap = [(0, 1), (1, 0)]

    def shift(held, step):
        return lax.ppermute(held, "x", [(i, (i + step) % count) for i in range(count)])

    arrived = [(shift(mine, step), -step) for step in (1, -1, 2)]
    grid = block_prefix.reshape(size["x"], size["zh"], size["y"], size["core"], tensor_count)
    grid = grid.transpose(0, 2, 1, 3, 4)

    def owner_of(offset, which):
        line = jnp.take(grid, (here + offset) % count, axis=0)
        return jnp.repeat(jnp.take(line, which, axis=2).reshape(-1), block_rows)

    everything = [(mine, 0)] + arrived
    own_rows = jnp.concatenate([held for held, _ in everything], axis=2)
    forwarded = lax.ppermute(own_rows, "core", swap)
    blocks = [(own_rows, jnp.concatenate([owner_of(offset, core) for _, offset in everything]))]
    blocks.append((forwarded, jnp.concatenate([owner_of(offset, 1 - core) for _, offset in everything])))
    return blocks


def fold_block(running, query_rows, keys, values, allowed):
    scores = jnp.einsum("thed,hpd->thep", query_rows, keys, preferred_element_type=jnp.float32)
    scores = jnp.where(allowed, scores * (1.0 / math.sqrt(HEAD)), masked_score)
    block_max = jnp.max(scores, axis=-1)
    if running is None:
        new_max = block_max
    else:
        old_max, old_total, old_sum = running
        new_max = jnp.maximum(old_max, block_max)
    weights = jnp.where(allowed, jnp.exp(scores - new_max[..., None]), 0.0)
    products = jnp.einsum(
        "thep,hpd->thed", weights.astype(jnp.bfloat16), values, preferred_element_type=jnp.float32
    )
    total = jnp.sum(weights, axis=-1)
    if running is not None:
        rescale = jnp.exp(old_max - new_max)
        total = old_total * rescale + total
        products = old_sum * rescale[..., None] + products
    return new_max, total, products


def token_layout(lengths, prefixes, slots):
    cumulative = jnp.cumsum(lengths)
    slot_ids = jnp.arange(slots, dtype=jnp.int32)
    request_ids = jnp.sum((slot_ids[:, None] >= cumulative[None, :]).astype(jnp.int32), axis=1)
    live_slots = slot_ids < cumulative[-1]
    onehot = request_ids[:, None] == jnp.arange(lengths.shape[0], dtype=jnp.int32)[None, :]
    token_group = jnp.sum(jnp.where(onehot, prefixes[None, :], 0), axis=1)
    return (slot_ids, request_ids, live_slots, token_group)


def per_device(
    queries, suffix_entries, prefix_cache, block_prefix, request_lengths, request_prefix
):
    tensor_count = lax.axis_size("tp")
    local_heads = HEADS // tensor_count
    token_rows = queries.shape[0]
    block_rows = prefix_cache.shape[0]
    column_count = prefix_cache.shape[1] // tensor_count
    slot_ids, request_ids, live_slots, token_group = token_layout(
        request_lengths, request_prefix, token_rows
    )
    halves = gather_cache(prefix_cache, block_prefix, tensor_count, local_heads)

    query_rows = queries.reshape(token_rows, local_heads, 2, HEAD)
    own_entries = suffix_entries.reshape(token_rows, local_heads, 2, HEAD)
    suffix_allowed = (
        (request_ids[:, None] == request_ids[None, :])
        & (slot_ids[None, :] <= slot_ids[:, None])
        & live_slots[:, None]
    )[:, None, None, :]
    own_keys = own_entries[:, :, 0].transpose(1, 0, 2)
    own_values = own_entries[:, :, 1].transpose(1, 0, 2)
    running = fold_block(None, query_rows, own_keys, own_values, suffix_allowed)
    for rows, owners in halves:
        allowed = ((token_group[:, None] == owners[None, :]) & live_slots[:, None])[:, None, None, :]
        running = fold_block(running, query_rows, rows[0], rows[1], allowed)
    row_max, total_weight, weighted = running
    live_grid = live_slots[:, None, None]
    safe_total = jnp.where(live_grid, total_weight, 1.0)
    result = jnp.where(live_grid[..., None], weighted / safe_total[..., None], 0.0)
    return result.astype(jnp.bfloat16).reshape(token_rows, local_heads * 2 * HEAD)


def solution(mesh):
    sizes = tuple(s for _, s in SEQ_PARTS) + (mesh.shape["tp"],)
    names = tuple(n for n, _ in SEQ_PARTS) + ("tp",)
    fine = Mesh(mesh.devices.reshape(sizes), names)
    seq = names[:-1]
    in_specs = (P(seq, "tp"), P(seq, "tp"), P(seq + ("tp",), None), P(), P(seq), P(seq))
    out_specs = P(seq, "tp")
    return jax.shard_map(
        per_device, mesh=fine, in_specs=in_specs, out_specs=out_specs, check_vma=False
    )
```

```python
import math

import jax
import jax.numpy as jnp
import numpy as np
from jax import lax
from jax.sharding import Mesh
from jax.sharding import PartitionSpec as P

HEADS = 16
HEAD = 128

masked_score = -1e30

SEQ_PARTS = (("x", 4), ("zh", 2), ("y", 8), ("core", 2))


def spread(held, axes, count):
    outgoing = jnp.broadcast_to(held[None], (count,) + held.shape)
    return lax.all_to_all(outgoing, axes, split_axis=0, concat_axis=3, tiled=True)[0]


def gather_cache(prefix_cache, block_prefix, tensor_count, local_heads):
    block_rows = prefix_cache.shape[0]
    size = dict(SEQ_PARTS)
    local = prefix_cache.reshape(block_rows, tensor_count, local_heads, 2, HEAD).transpose(1, 3, 2, 0, 4)
    lines = size["y"] * size["zh"]
    outgoing = jnp.broadcast_to(local[None], (lines,) + local.shape)
    outgoing = outgoing.reshape((lines * tensor_count,) + local.shape[1:])
    mine = lax.all_to_all(outgoing, ("y", "zh", "tp"), split_axis=0, concat_axis=3, tiled=True)[0]
    count = size["x"]
    here = lax.axis_index("x")
    core = lax.axis_index("core")
    swap = [(0, 1), (1, 0)]

    def shift(held, step):
        return lax.ppermute(held, "x", [(i, (i + step) % count) for i in range(count)])

    arrived = [(shift(mine, step), -step) for step in (2, 1, -1)]
    grid = block_prefix.reshape(size["x"], size["zh"], size["y"], size["core"], tensor_count)
    grid = grid.transpose(0, 2, 1, 3, 4)

    def owner_of(offset, which):
        line = jnp.take(grid, (here + offset) % count, axis=0)
        return jnp.repeat(jnp.take(line, which, axis=2).reshape(-1), block_rows)

    blocks = [(mine, owner_of(0, core))]
    blocks += [(held, owner_of(offset, core)) for held, offset in arrived]
    everything = [(mine, 0)] + arrived
    forwarded = lax.ppermute(jnp.concatenate([held for held, _ in everything], axis=2), "core", swap)
    blocks.append((forwarded, jnp.concatenate([owner_of(offset, 1 - core) for _, offset in everything])))
    return blocks


def fold_block(running, query_rows, keys, values, allowed):
    scores = jnp.einsum("thed,hpd->thep", query_rows, keys, preferred_element_type=jnp.float32)
    scores = jnp.where(allowed, scores * (1.0 / math.sqrt(HEAD)), masked_score)
    block_max = jnp.max(scores, axis=-1)
    if running is None:
        new_max = block_max
    else:
        old_max, old_total, old_sum = running
        new_max = jnp.maximum(old_max, block_max)
    weights = jnp.where(allowed, jnp.exp(scores - new_max[..., None]), 0.0)
    products = jnp.einsum(
        "thep,hpd->thed", weights.astype(jnp.bfloat16), values, preferred_element_type=jnp.float32
    )
    total = jnp.sum(weights, axis=-1)
    if running is not None:
        rescale = jnp.exp(old_max - new_max)
        total = old_total * rescale + total
        products = old_sum * rescale[..., None] + products
    return new_max, total, products


def token_layout(lengths, prefixes, slots):
    cumulative = jnp.cumsum(lengths)
    slot_ids = jnp.arange(slots, dtype=jnp.int32)
    request_ids = jnp.sum((slot_ids[:, None] >= cumulative[None, :]).astype(jnp.int32), axis=1)
    live_slots = slot_ids < cumulative[-1]
    onehot = request_ids[:, None] == jnp.arange(lengths.shape[0], dtype=jnp.int32)[None, :]
    token_group = jnp.sum(jnp.where(onehot, prefixes[None, :], 0), axis=1)
    return (slot_ids, request_ids, live_slots, token_group)


def per_device(
    queries, suffix_entries, prefix_cache, block_prefix, request_lengths, request_prefix
):
    tensor_count = lax.axis_size("tp")
    local_heads = HEADS // tensor_count
    token_rows = queries.shape[0]
    block_rows = prefix_cache.shape[0]
    column_count = prefix_cache.shape[1] // tensor_count
    slot_ids, request_ids, live_slots, token_group = token_layout(
        request_lengths, request_prefix, token_rows
    )
    halves = gather_cache(prefix_cache, block_prefix, tensor_count, local_heads)

    query_rows = queries.reshape(token_rows, local_heads, 2, HEAD)
    own_entries = suffix_entries.reshape(token_rows, local_heads, 2, HEAD)
    suffix_allowed = (
        (request_ids[:, None] == request_ids[None, :])
        & (slot_ids[None, :] <= slot_ids[:, None])
        & live_slots[:, None]
    )[:, None, None, :]
    own_keys = own_entries[:, :, 0].transpose(1, 0, 2)
    own_values = own_entries[:, :, 1].transpose(1, 0, 2)
    running = fold_block(None, query_rows, own_keys, own_values, suffix_allowed)
    for rows, owners in halves:
        allowed = ((token_group[:, None] == owners[None, :]) & live_slots[:, None])[:, None, None, :]
        running = fold_block(running, query_rows, rows[0], rows[1], allowed)
    row_max, total_weight, weighted = running
    live_grid = live_slots[:, None, None]
    safe_total = jnp.where(live_grid, total_weight, 1.0)
    result = jnp.where(live_grid[..., None], weighted / safe_total[..., None], 0.0)
    return result.astype(jnp.bfloat16).reshape(token_rows, local_heads * 2 * HEAD)


def solution(mesh):
    sizes = tuple(s for _, s in SEQ_PARTS) + (mesh.shape["tp"],)
    names = tuple(n for n, _ in SEQ_PARTS) + ("tp",)
    fine = Mesh(mesh.devices.reshape(sizes), names)
    seq = names[:-1]
    in_specs = (P(seq, "tp"), P(seq, "tp"), P(seq + ("tp",), None), P(), P(seq), P(seq))
    out_specs = P(seq, "tp")
    return jax.shard_map(
        per_device, mesh=fine, in_specs=in_specs, out_specs=out_specs, check_vma=False
    )
```

```python
import math

import jax
import jax.numpy as jnp
import numpy as np
from jax import lax
from jax.sharding import Mesh
from jax.sharding import PartitionSpec as P

HEADS = 16
HEAD = 128

masked_score = -1e30

SEQ_PARTS = (("x", 4), ("zh", 2), ("y", 8), ("core", 2))


def spread(held, axes, count):
    outgoing = jnp.broadcast_to(held[None], (count,) + held.shape)
    return lax.all_to_all(outgoing, axes, split_axis=0, concat_axis=3, tiled=True)[0]


def gather_cache(prefix_cache, block_prefix, tensor_count, local_heads):
    block_rows = prefix_cache.shape[0]
    size = dict(SEQ_PARTS)
    local = prefix_cache.reshape(block_rows, tensor_count, local_heads, 2, HEAD).transpose(1, 3, 2, 0, 4)
    lines = size["y"] * size["zh"]
    outgoing = jnp.broadcast_to(local[None], (lines,) + local.shape)
    outgoing = outgoing.reshape((lines * tensor_count,) + local.shape[1:])
    mine = lax.all_to_all(outgoing, ("y", "zh", "tp"), split_axis=0, concat_axis=3, tiled=True)[0]
    count = size["x"]
    here = lax.axis_index("x")
    core = lax.axis_index("core")
    swap = [(0, 1), (1, 0)]

    def shift(held, step):
        return lax.ppermute(held, "x", [(i, (i + step) % count) for i in range(count)])

    arrived = [(shift(mine, step), -step) for step in (-1, 1, 2)]
    grid = block_prefix.reshape(size["x"], size["zh"], size["y"], size["core"], tensor_count)
    grid = grid.transpose(0, 2, 1, 3, 4)

    def owner_of(offset, which):
        line = jnp.take(grid, (here + offset) % count, axis=0)
        return jnp.repeat(jnp.take(line, which, axis=2).reshape(-1), block_rows)

    blocks = [(mine, owner_of(0, core))]
    blocks += [(held, owner_of(offset, core)) for held, offset in arrived]
    everything = [(mine, 0)] + arrived
    forwarded = lax.ppermute(jnp.concatenate([held for held, _ in everything], axis=2), "core", swap)
    blocks.append((forwarded, jnp.concatenate([owner_of(offset, 1 - core) for _, offset in everything])))
    return blocks


def fold_block(running, query_rows, keys, values, allowed):
    scores = jnp.einsum("thed,hpd->thep", query_rows, keys, preferred_element_type=jnp.float32)
    scores = jnp.where(allowed, scores * (1.0 / math.sqrt(HEAD)), masked_score)
    block_max = jnp.max(scores, axis=-1)
    if running is None:
        new_max = block_max
    else:
        old_max, old_total, old_sum = running
        new_max = jnp.maximum(old_max, block_max)
    weights = jnp.where(allowed, jnp.exp(scores - new_max[..., None]), 0.0)
    products = jnp.einsum(
        "thep,hpd->thed", weights.astype(jnp.bfloat16), values, preferred_element_type=jnp.float32
    )
    total = jnp.sum(weights, axis=-1)
    if running is not None:
        rescale = jnp.exp(old_max - new_max)
        total = old_total * rescale + total
        products = old_sum * rescale[..., None] + products
    return new_max, total, products


def token_layout(lengths, prefixes, slots):
    cumulative = jnp.cumsum(lengths)
    slot_ids = jnp.arange(slots, dtype=jnp.int32)
    request_ids = jnp.sum((slot_ids[:, None] >= cumulative[None, :]).astype(jnp.int32), axis=1)
    live_slots = slot_ids < cumulative[-1]
    onehot = request_ids[:, None] == jnp.arange(lengths.shape[0], dtype=jnp.int32)[None, :]
    token_group = jnp.sum(jnp.where(onehot, prefixes[None, :], 0), axis=1)
    return (slot_ids, request_ids, live_slots, token_group)


def per_device(
    queries, suffix_entries, prefix_cache, block_prefix, request_lengths, request_prefix
):
    tensor_count = lax.axis_size("tp")
    local_heads = HEADS // tensor_count
    token_rows = queries.shape[0]
    block_rows = prefix_cache.shape[0]
    column_count = prefix_cache.shape[1] // tensor_count
    slot_ids, request_ids, live_slots, token_group = token_layout(
        request_lengths, request_prefix, token_rows
    )
    halves = gather_cache(prefix_cache, block_prefix, tensor_count, local_heads)

    query_rows = queries.reshape(token_rows, local_heads, 2, HEAD)
    own_entries = suffix_entries.reshape(token_rows, local_heads, 2, HEAD)
    suffix_allowed = (
        (request_ids[:, None] == request_ids[None, :])
        & (slot_ids[None, :] <= slot_ids[:, None])
        & live_slots[:, None]
    )[:, None, None, :]
    own_keys = own_entries[:, :, 0].transpose(1, 0, 2)
    own_values = own_entries[:, :, 1].transpose(1, 0, 2)
    running = fold_block(None, query_rows, own_keys, own_values, suffix_allowed)
    for rows, owners in halves:
        allowed = ((token_group[:, None] == owners[None, :]) & live_slots[:, None])[:, None, None, :]
        running = fold_block(running, query_rows, rows[0], rows[1], allowed)
    row_max, total_weight, weighted = running
    live_grid = live_slots[:, None, None]
    safe_total = jnp.where(live_grid, total_weight, 1.0)
    result = jnp.where(live_grid[..., None], weighted / safe_total[..., None], 0.0)
    return result.astype(jnp.bfloat16).reshape(token_rows, local_heads * 2 * HEAD)


def solution(mesh):
    sizes = tuple(s for _, s in SEQ_PARTS) + (mesh.shape["tp"],)
    names = tuple(n for n, _ in SEQ_PARTS) + ("tp",)
    fine = Mesh(mesh.devices.reshape(sizes), names)
    seq = names[:-1]
    in_specs = (P(seq, "tp"), P(seq, "tp"), P(seq + ("tp",), None), P(), P(seq), P(seq))
    out_specs = P(seq, "tp")
    return jax.shard_map(
        per_device, mesh=fine, in_specs=in_specs, out_specs=out_specs, check_vma=False
    )
```
